256 devices in a mesh: section: 32 (over z_hi, y, core), tensor: 8 (over z_lo, x).
Axes of the slice: x: 4, y: 4, z: 8 (z_hi: 4, z_lo: 2; z = z_hi * 2 + z_lo), core: 2. Of those that a mesh axis runs over, the one named last changes fastest.
Arguments:
- acts: bfloat16 [32, 512, 3072], P('section', 'tensor'), may hold values from -6 to 6
- sides: bfloat16 [32, 512, 3072], P('section', 'tensor'), may hold values from -6 to 6
- gains: float32 [32, 3072], P('section'), may hold values from 0.1 to 1.9
- weights: bfloat16 [32, 6144, 3072], P('section', None, 'tensor'), may hold values from -0.078125 to 0.078125
- back_acts: bfloat16 [32, 512, 3072], P('section', 'tensor'), may hold values from -6 to 6
- back_sides: bfloat16 [32, 512, 3072], P('section', 'tensor'), may hold values from -6 to 6
- back_grads: bfloat16 [32, 512, 3072], P('section', 'tensor'), may hold values from -6 to 6
Outputs:
- received: bfloat16 [32, 512, 3072], P('section', 'tensor')
- mirrored: bfloat16 [32, 512, 3072], P('section', 'tensor')
- grad_received: bfloat16 [32, 512, 3072], P('section', 'tensor')
- weight_grads: bfloat16 [32, 6144, 3072], P('section', None, 'tensor')
- gain_grads: float32 [32, 3072], P('section')
The draws below stay inside these ranges and needn't reach their ends.
All inputs are finite; a program needn't handle non-finite values.
Results may differ from the reference program's by a relative error of at most 0.015.
Values may be sent and summed in bfloat16 or wider, within the bound.
No kernel may reach another device: no remote copies, remote signals or barrier semaphores. Data moves between devices by JAX's collectives and lax.ppermute only.
A program may use at most 128 MiB of HBM per device.

```python
import jax
import jax.numpy as jnp
from jax import lax

D = 3072
TOK_MB = 512
SECTIONS = 32
HALF = 16
N_TENSOR = 8


def levels(key, dims, cuts, low, largest):
    factor_of, own = 1.0, jax.random.fold_in(key, 6)
    for dim, shards_of in cuts:
        heights = jnp.exp(jax.random.uniform(jax.random.fold_in(own, dim), (shards_of,), jnp.float32, low / len(cuts), largest / len(cuts)))
        factor_of = factor_of * jnp.repeat(heights, dims[dim] // shards_of).reshape([-1 if axis == dim else 1 for axis in range(len(dims))])
    return factor_of


def noise(own_key, shape, deviation, most, split=(), held_as=jnp.bfloat16):
    result = jax.random.normal(own_key, shape, jnp.float32) * deviation
    if len(split) > 0:
        result = levels(own_key, shape, split, -0.22, 0.18) * result
    return jnp.clip(result, min=-most, max=most).astype(held_as)


def setup_inputs(seed: int = 0) -> dict:
    splits = jax.random.split(jax.random.key(seed), 8)
    return {
        "acts": noise(splits[0], (SECTIONS, TOK_MB, D), 1.0, 6.0, ((0, 32), (1, 8))),
        "sides": noise(splits[1], (SECTIONS, TOK_MB, D), 1.0, 6.0, ((0, 32), (1, 8))),
        "gains": jnp.clip(1.0 + 0.18 * jax.random.normal(splits[2], (SECTIONS, D), jnp.float32), 0.1, 1.9),
        "weights": noise(splits[3], (SECTIONS, 2 * D, D), (2 * D) ** -0.5, 0.078125, ((0, 32), (2, 8))),
        "back_acts": noise(splits[4], (SECTIONS, TOK_MB, D), 1.0, 6.0, ((0, 32), (1, 8))),
        "back_sides": noise(splits[5], (SECTIONS, TOK_MB, D), 1.0, 6.0, ((0, 32), (1, 8))),
        "back_grads": noise(splits[6], (SECTIONS, TOK_MB, D), 1.0, 6.0, ((0, 32), (1, 8))),
    }


epsilon = 1e-06
tanh_scale = 0.7978845608028654
cubic_term = 0.044715

def gelu_value(inputs):
    inside = tanh_scale * (inputs + cubic_term * inputs * inputs * inputs)
    return 0.5 * inputs * (1.0 + jnp.tanh(inside))

def gelu_slope(inputs):
    inside = tanh_scale * (inputs + cubic_term * inputs * inputs * inputs)
    bent = jnp.tanh(inside)
    return 0.5 * (1.0 + bent) + 0.5 * inputs * (1.0 - bent * bent) * tanh_scale * (1.0 + 3.0 * cubic_term * inputs * inputs)

def normalize(rows_in, gain):
    xfloat = rows_in.astype(jnp.float32)
    rinv = lax.rsqrt(lax.optimization_barrier(jnp.mean(xfloat * xfloat, axis=-1, keepdims=True)) + epsilon)
    return (xfloat, rinv, (xfloat * rinv * gain).astype(jnp.bfloat16))

def reference(acts, sides, gains, weights, back_acts, back_sides, back_grads):
    sections = SECTIONS
    middle = HALF
    block_cols = D // N_TENSOR
    out_list = []
    dx_list = []
    payload_list = []
    weight_list = []
    gain_list = []
    for section_idx in range(sections):
        gain = gains[section_idx]
        weight_all = weights[section_idx]
        xfloat, rinv, normed = normalize(acts[section_idx], gain)
        joined = jnp.concatenate([normed, sides[section_idx]], axis=1)
        hidden = jnp.dot(joined, weight_all, preferred_element_type=jnp.float32)
        out_rows = (xfloat + gelu_value(hidden)).astype(jnp.bfloat16)
        out_list.append(out_rows)
        bfloat, brinv, bnormed = normalize(back_acts[section_idx], gain)
        bfused = jnp.concatenate([bnormed, back_sides[section_idx]], axis=1)
        bhidden = jnp.dot(bfused, weight_all, preferred_element_type=jnp.float32)
        incoming = back_grads[section_idx].astype(jnp.float32)
        dhidden = (incoming * gelu_slope(bhidden)).astype(jnp.bfloat16)
        weight_list.append(jnp.dot(bfused.T, dhidden, preferred_element_type=jnp.float32).astype(jnp.bfloat16))
        dfused = jnp.zeros((TOK_MB, 2 * D), jnp.float32)
        for block_idx in range(N_TENSOR):
            low = block_idx * block_cols
            part_term = jnp.dot(dhidden[:, low:low + block_cols], weight_all[:, low:low + block_cols].T, preferred_element_type=jnp.float32)
            rounded = lax.optimization_barrier(part_term.astype(jnp.bfloat16))
            dfused = dfused + rounded.astype(jnp.float32)
        dnormed = dfused[:, :D]
        dside = dfused[:, D:].astype(jnp.bfloat16)
        gain_list.append(lax.optimization_barrier(jnp.sum(dnormed * bfloat * brinv, axis=0)))
        scaled = gain * dnormed
        dnorm_in = brinv * scaled - bfloat * brinv * brinv * brinv * lax.optimization_barrier(jnp.mean(scaled * bfloat, axis=-1, keepdims=True))
        dx_list.append((incoming + dnorm_in).astype(jnp.bfloat16))
        payload_list.append(out_rows if section_idx < middle else dside)
    outs = jnp.stack(out_list)
    received = jnp.roll(outs, 1, axis=0)
    grad_received = jnp.roll(jnp.stack(dx_list), -1, axis=0)
    mirrored = jnp.stack(payload_list)[::-1]
    weight_grads = jnp.stack(weight_list)
    gain_grads = jnp.stack(gain_list)
    return (received, mirrored, grad_received, weight_grads, gain_grads)
```

```python
import jax
import jax.numpy as jnp
from jax import lax
from jax.sharding import PartitionSpec as P

epsilon = 1e-06
tanh_scale = 0.7978845608028654
cubic_term = 0.044715


def shifted(block, axis, distance):
    devices = range(lax.axis_size(axis))
    route = [((i - distance) % len(devices), i) for i in devices]
    return lax.ppermute(block, axis, route)


def gelu_value(inputs):
    inside = tanh_scale * (inputs + cubic_term * inputs * inputs * inputs)
    return 0.5 * inputs * (1.0 + jnp.tanh(inside))


def gelu_slope(inputs):
    inside = tanh_scale * (inputs + cubic_term * inputs * inputs * inputs)
    bent = jnp.tanh(inside)
    return 0.5 * (1.0 + bent) + 0.5 * inputs * (1.0 - bent * bent) * tanh_scale * (
        1.0 + 3.0 * cubic_term * inputs * inputs
    )


def normalize(rows_in, gain):
    xfloat = rows_in.astype(jnp.float32)
    rinv = lax.rsqrt(jnp.mean(xfloat * xfloat, axis=-1, keepdims=True) + epsilon)
    return (xfloat, rinv, (xfloat * rinv * gain).astype(jnp.bfloat16))


def gathered(block, axis):
    count = lax.axis_size(axis)
    copies = jnp.broadcast_to(block[None], (count,) + block.shape)
    copies = copies.reshape(count * block.shape[0], block.shape[1])
    return lax.all_to_all(copies, axis, 0, 0, tiled=True)


def on_device(acts, sides, gains, weights, back_acts, back_sides, back_grads):
    sections = lax.axis_size("section")
    count = lax.axis_size("tensor")
    middle = sections // 2
    section_idx = lax.axis_index("section")
    gain = gains[0]
    weight_all = weights[0]
    rows, width = acts[0].shape

    xfloat, rinv, normed = normalize(acts[0], gain)
    joined_all = gathered(jnp.concatenate([normed, sides[0]], axis=1), "tensor")
    hidden = jnp.dot(joined_all, weight_all, preferred_element_type=jnp.float32)
    update = lax.all_to_all(
        gelu_value(hidden).astype(jnp.bfloat16), "tensor", split_axis=0, concat_axis=1, tiled=True
    ).astype(jnp.float32)
    out_rows = (xfloat + update).astype(jnp.bfloat16)
    received = shifted(out_rows, "section", 1)
    ahead = lax.ppermute(
        out_rows, "section", [(s, sections - 1 - s) for s in range(middle)]
    )

    raw_all = gathered(jnp.concatenate([back_acts[0], back_sides[0]], axis=1), "tensor")
    bfloat_all, brinv_all, bnormed_all = normalize(raw_all[:, :width], gain)
    bfused_all = jnp.concatenate([bnormed_all, raw_all[:, width:]], axis=1)
    bhidden = jnp.dot(bfused_all, weight_all, preferred_element_type=jnp.float32)
    grad_cols = lax.all_to_all(back_grads[0], "tensor", split_axis=1, concat_axis=0, tiled=True)
    dhidden = (grad_cols.astype(jnp.float32) * gelu_slope(bhidden)).astype(jnp.bfloat16)
    contract = (((0,), (0,)), ((), ()))
    weight_grads = lax.dot_general(
        bfused_all, dhidden, contract, preferred_element_type=jnp.float32
    ).astype(jnp.bfloat16)
    across = (((1,), (1,)), ((), ()))
    term = lax.dot_general(
        dhidden, weight_all, across, preferred_element_type=jnp.float32
    ).astype(jnp.bfloat16)
    gain_part = jnp.sum(term[:, :width].astype(jnp.float32) * bfloat_all * brinv_all, axis=0)
    part_hi = gain_part.astype(jnp.bfloat16)
    part_lo = (gain_part - part_hi.astype(jnp.float32)).astype(jnp.bfloat16)
    extra = jnp.concatenate([part_hi, part_lo])[None, None]
    send = jnp.concatenate(
        [term.reshape(count, rows, 2 * width), jnp.broadcast_to(extra, (count, 1, 2 * width))], axis=1
    ).reshape(count * (rows + 1), 2 * width)
    got = lax.all_to_all(send, "tensor", 0, 0, tiled=True).reshape(count, rows + 1, 2 * width)
    dfused = jnp.sum(got[:, :rows].astype(jnp.float32), axis=0)
    shares = got[:, rows].astype(jnp.float32)
    gain_grad = jnp.sum(shares[:, :width] + shares[:, width:], axis=0)
    dnormed = dfused[:, :width]
    dside = dfused[:, width:].astype(jnp.bfloat16)
    bfloat, brinv, _ = normalize(back_acts[0], gain)
    scaled = gain * dnormed
    dnorm_in = brinv * scaled - bfloat * brinv * brinv * brinv * jnp.mean(
        scaled * bfloat, axis=-1, keepdims=True
    )
    dx_rows = (back_grads[0].astype(jnp.float32) + dnorm_in).astype(jnp.bfloat16)
    grad_received = shifted(dx_rows, "section", -1)
    behind = lax.ppermute(
        dside, "section", [(s, sections - 1 - s) for s in range(middle, sections)]
    )
    mirrored = jnp.where(section_idx >= middle, ahead, behind)
    return (
        received[None],
        mirrored[None],
        grad_received[None],
        weight_grads[None],
        gain_grad[None],
    )


def solution(mesh):
    placed = (
        P("section", "tensor", None),
        P("section", "tensor", None),
        P("section", None),
        P("section", None, "tensor"),
        P("section", "tensor", None),
        P("section", "tensor", None),
        P("section", "tensor", None),
    )
    return jax.shard_map(
        on_device,
        mesh=mesh,
        in_specs=placed,
        out_specs=(
            P("section", "tensor", None),
            P("section", "tensor", None),
            P("section", "tensor", None),
            P("section", None, "tensor"),
            P("section", None),
        ),
        check_vma=False,
    )
```

```python
import jax
import jax.numpy as jnp
from jax import lax
from jax.sharding import PartitionSpec as P

epsilon = 1e-06
tanh_scale = 0.7978845608028654
cubic_term = 0.044715


def shifted(block, axis, distance):
    devices = range(lax.axis_size(axis))
    route = [((i - distance) % len(devices), i) for i in devices]
    return lax.ppermute(block, axis, route)


def gelu_value(inputs):
    inside = tanh_scale * (inputs + cubic_term * inputs * inputs * inputs)
    return 0.5 * inputs * (1.0 + jnp.tanh(inside))


def gelu_slope(inputs):
    inside = tanh_scale * (inputs + cubic_term * inputs * inputs * inputs)
    bent = jnp.tanh(inside)
    return 0.5 * (1.0 + bent) + 0.5 * inputs * (1.0 - bent * bent) * tanh_scale * (
        1.0 + 3.0 * cubic_term * inputs * inputs
    )


def normalize(rows_in, gain):
    xfloat = rows_in.astype(jnp.float32)
    rinv = lax.rsqrt(jnp.mean(xfloat * xfloat, axis=-1, keepdims=True) + epsilon)
    return (xfloat, rinv, (xfloat * rinv * gain).astype(jnp.bfloat16))


def gathered(block, axis):
    count = lax.axis_size(axis)
    copies = jnp.broadcast_to(block[None], (count,) + block.shape)
    copies = copies.reshape(count * block.shape[0], block.shape[1])
    return lax.all_to_all(copies, axis, 0, 0, tiled=True)


def on_device(acts, sides, gains, weights, back_acts, back_sides, back_grads):
    sections = lax.axis_size("section")
    count = lax.axis_size("tensor")
    middle = sections // 2
    section_idx = lax.axis_index("section")
    gain = gains[0]
    weight_all = weights[0]
    rows, width = acts[0].shape

    raw_all = gathered(jnp.concatenate([back_acts[0], back_sides[0]], axis=1), "tensor")
    xfloat, rinv, normed = normalize(acts[0], gain)
    joined = jnp.concatenate([normed, sides[0]], axis=1)
    raw_all, joined = lax.optimization_barrier((raw_all, joined))
    joined_all = gathered(joined, "tensor")
    bfloat_all, brinv_all, bnormed_all = normalize(raw_all[:, :width], gain)
    bfused_all = jnp.concatenate([bnormed_all, raw_all[:, width:]], axis=1)
    bhidden = jnp.dot(bfused_all, weight_all, preferred_element_type=jnp.float32)
    grad_cols = lax.all_to_all(back_grads[0], "tensor", split_axis=1, concat_axis=0, tiled=True)
    dhidden = (grad_cols.astype(jnp.float32) * gelu_slope(bhidden)).astype(jnp.bfloat16)
    contract = (((0,), (0,)), ((), ()))
    weight_grads = lax.dot_general(
        bfused_all, dhidden, contract, preferred_element_type=jnp.float32
    ).astype(jnp.bfloat16)
    across = (((1,), (1,)), ((), ()))
    term = lax.dot_general(
        dhidden, weight_all, across, preferred_element_type=jnp.float32
    ).astype(jnp.bfloat16)
    gain_part = jnp.sum(term[:, :width].astype(jnp.float32) * bfloat_all * brinv_all, axis=0)
    part_hi = gain_part.astype(jnp.bfloat16)
    part_lo = (gain_part - part_hi.astype(jnp.float32)).astype(jnp.bfloat16)
    extra = jnp.concatenate([part_hi, part_lo])[None, None]
    send = jnp.concatenate(
        [term.reshape(count, rows, 2 * width), jnp.broadcast_to(extra, (count, 1, 2 * width))], axis=1
    ).reshape(count * (rows + 1), 2 * width)
    got = lax.all_to_all(send, "tensor", 0, 0, tiled=True).reshape(count, rows + 1, 2 * width)

    hidden = jnp.dot(joined_all, weight_all, preferred_element_type=jnp.float32)
    update = lax.all_to_all(
        gelu_value(hidden).astype(jnp.bfloat16), "tensor", split_axis=0, concat_axis=1, tiled=True
    ).astype(jnp.float32)
    out_rows = (xfloat + update).astype(jnp.bfloat16)
    received = shifted(out_rows, "section", 1)
    ahead = lax.ppermute(
        out_rows, "section", [(s, sections - 1 - s) for s in range(middle)]
    )

    dfused = jnp.sum(got[:, :rows].astype(jnp.float32), axis=0)
    shares = got[:, rows].astype(jnp.float32)
    gain_grad = jnp.sum(shares[:, :width] + shares[:, width:], axis=0)
    dnormed = dfused[:, :width]
    dside = dfused[:, width:].astype(jnp.bfloat16)
    bfloat, brinv, _ = normalize(back_acts[0], gain)
    scaled = gain * dnormed
    dnorm_in = brinv * scaled - bfloat * brinv * brinv * brinv * jnp.mean(
        scaled * bfloat, axis=-1, keepdims=True
    )
    dx_rows = (back_grads[0].astype(jnp.float32) + dnorm_in).astype(jnp.bfloat16)
    grad_received = shifted(dx_rows, "section", -1)
    behind = lax.ppermute(
        dside, "section", [(s, sections - 1 - s) for s in range(middle, sections)]
    )
    mirrored = jnp.where(section_idx >= middle, ahead, behind)
    return (
        received[None],
        mirrored[None],
        grad_received[None],
        weight_grads[None],
        gain_grad[None],
    )


def solution(mesh):
    placed = (
        P("section", "tensor", None),
        P("section", "tensor", None),
        P("section", None),
        P("section", None, "tensor"),
        P("section", "tensor", None),
        P("section", "tensor", None),
        P("section", "tensor", None),
    )
    return jax.shard_map(
        on_device,
        mesh=mesh,
        in_specs=placed,
        out_specs=(
            P("section", "tensor", None),
            P("section", "tensor", None),
            P("section", "tensor", None),
            P("section", None, "tensor"),
            P("section", None),
        ),
        check_vma=False,
    )
```

```python
import jax
import jax.numpy as jnp
from jax import lax
from jax.sharding import PartitionSpec as P

epsilon = 1e-06
tanh_scale = 0.7978845608028654
cubic_term = 0.044715


def shifted(block, axis, distance):
    devices = range(lax.axis_size(axis))
    route = [((i - distance) % len(devices), i) for i in devices]
    return lax.ppermute(block, axis, route)


def gelu_value(inputs):
    inside = tanh_scale * (inputs + cubic_term * inputs * inputs * inputs)
    return 0.5 * inputs * (1.0 + jnp.tanh(inside))


def gelu_slope(inputs):
    inside = tanh_scale * (inputs + cubic_term * inputs * inputs * inputs)
    bent = jnp.tanh(inside)
    return 0.5 * (1.0 + bent) + 0.5 * inputs * (1.0 - bent * bent) * tanh_scale * (
        1.0 + 3.0 * cubic_term * inputs * inputs
    )


def normalize(rows_in, gain):
    xfloat = rows_in.astype(jnp.float32)
    rinv = lax.rsqrt(jnp.mean(xfloat * xfloat, axis=-1, keepdims=True) + epsilon)
    return (xfloat, rinv, (xfloat * rinv * gain).astype(jnp.bfloat16))


def spread(block, count):
    return jnp.broadcast_to(block[None], (count,) + block.shape)


def exchange(chunks, axis):
    count, rows, cols = chunks.shape
    got = lax.all_to_all(chunks.reshape(count * rows, cols), axis, 0, 0, tiled=True)
    return got.reshape(count, rows, cols)


def on_device(acts, sides, gains, weights, back_acts, back_sides, back_grads):
    sections = lax.axis_size("section")
    count = lax.axis_size("tensor")
    middle = sections // 2
    section_idx = lax.axis_index("section")
    gain = gains[0]
    weight_all = weights[0]
    rows, width = acts[0].shape
    block_cols = weight_all.shape[1]
    lanes = 128
    gain_rows = 2 * width // lanes

    grad_blocks = back_grads[0].reshape(rows, count, block_cols).transpose(1, 0, 2)
    raw = jnp.concatenate([back_acts[0], back_sides[0]], axis=1)
    got_b = exchange(jnp.concatenate([spread(raw, count), grad_blocks], axis=2), "tensor")
    xfloat, _, normed = normalize(acts[0], gain)
    chunks_f = spread(jnp.concatenate([normed, sides[0]], axis=1), count)
    got_b, chunks_f = lax.optimization_barrier((got_b, chunks_f))
    joined_all = exchange(chunks_f, "tensor").reshape(count * rows, 2 * width)

    raw_all = got_b[:, :, : 2 * width].reshape(count * rows, 2 * width)
    grad_cols = got_b[:, :, 2 * width :].reshape(count * rows, block_cols)
    bfloat_all, brinv_all, bnormed_all = normalize(raw_all[:, :width], gain)
    bfused_all = jnp.concatenate([bnormed_all, raw_all[:, width:]], axis=1)
    bhidden = jnp.dot(bfused_all, weight_all, preferred_element_type=jnp.float32)
    dhidden = (grad_cols.astype(jnp.float32) * gelu_slope(bhidden)).astype(jnp.bfloat16)
    contract = (((0,), (0,)), ((), ()))
    weight_grads = lax.dot_general(
        bfused_all, dhidden, contract, preferred_element_type=jnp.float32
    ).astype(jnp.bfloat16)
    across = (((1,), (1,)), ((), ()))
    term = lax.dot_general(
        dhidden, weight_all, across, preferred_element_type=jnp.float32
    ).astype(jnp.bfloat16)
    gain_part = jnp.sum(term[:, :width].astype(jnp.float32) * bfloat_all * brinv_all, axis=0)
    part_hi = gain_part.astype(jnp.bfloat16)
    part_lo = (gain_part - part_hi.astype(jnp.float32)).astype(jnp.bfloat16)
    gain_tile = jnp.concatenate([part_hi, part_lo]).reshape(gain_rows, lanes)
    gain_tile = jnp.pad(gain_tile, ((0, rows - gain_rows), (0, 0)))

    hidden = jnp.dot(joined_all, weight_all, preferred_element_type=jnp.float32)
    update = gelu_value(hidden).astype(jnp.bfloat16)

    chunks = jnp.concatenate(
        [
            term.reshape(count, rows, 2 * width),
            update.reshape(count, rows, block_cols),
            jnp.broadcast_to(gain_tile[None], (count, rows, lanes)),
        ],
        axis=2,
    )
    got = exchange(chunks, "tensor")
    dfused = jnp.sum(got[:, :, : 2 * width].astype(jnp.float32), axis=0)
    update_rows = got[:, :, 2 * width : 2 * width + block_cols].transpose(1, 0, 2).reshape(rows, width)
    shares = got[:, :gain_rows, 2 * width + block_cols :].reshape(count, 2 * width).astype(jnp.float32)
    gain_grad = jnp.sum(shares[:, :width] + shares[:, width:], axis=0)

    out_rows = (xfloat + update_rows.astype(jnp.float32)).astype(jnp.bfloat16)
    received = shifted(out_rows, "section", 1)
    dnormed = dfused[:, :width]
    dside = dfused[:, width:].astype(jnp.bfloat16)
    bfloat, brinv, _ = normalize(back_acts[0], gain)
    scaled = gain * dnormed
    dnorm_in = brinv * scaled - bfloat * brinv * brinv * brinv * jnp.mean(
        scaled * bfloat, axis=-1, keepdims=True
    )
    dx_rows = (back_grads[0].astype(jnp.float32) + dnorm_in).astype(jnp.bfloat16)
    grad_received = shifted(dx_rows, "section", -1)
    payload = jnp.where(section_idx < middle, out_rows, dside)
    mirrored = lax.ppermute(payload, "section", [(s, sections - 1 - s) for s in range(sections)])
    return (
        received[None],
        mirrored[None],
        grad_received[None],
        weight_grads[None],
        gain_grad[None],
    )


def solution(mesh):
    placed = (
        P("section", "tensor", None),
        P("section", "tensor", None),
        P("section", None),
        P("section", None, "tensor"),
        P("section", "tensor", None),
        P("section", "tensor", None),
        P("section", "tensor", None),
    )
    return jax.shard_map(
        on_device,
        mesh=mesh,
        in_specs=placed,
        out_specs=(
            P("section", "tensor", None),
            P("section", "tensor", None),
            P("section", "tensor", None),
            P("section", None, "tensor"),
            P("section", None),
        ),
        check_vma=False,
    )
```

```python
import jax
import jax.numpy as jnp
from jax import lax
from jax.sharding import PartitionSpec as P

epsilon = 1e-06
tanh_scale = 0.7978845608028654
cubic_term = 0.044715


def shifted(block, axis, distance):
    devices = range(lax.axis_size(axis))
    route = [((i - distance) % len(devices), i) for i in devices]
    return lax.ppermute(block, axis, route)


def gelu_value(inputs):
    inside = tanh_scale * (inputs + cubic_term * inputs * inputs * inputs)
    return 0.5 * inputs * (1.0 + jnp.tanh(inside))


def gelu_slope(inputs):
    inside = tanh_scale * (inputs + cubic_term * inputs * inputs * inputs)
    bent = jnp.tanh(inside)
    return 0.5 * (1.0 + bent) + 0.5 * inputs * (1.0 - bent * bent) * tanh_scale * (
        1.0 + 3.0 * cubic_term * inputs * inputs
    )


def normalize(rows_in, gain):
    xfloat = rows_in.astype(jnp.float32)
    rinv = lax.rsqrt(jnp.mean(xfloat * xfloat, axis=-1, keepdims=True) + epsilon)
    return (xfloat, rinv, (xfloat * rinv * gain).astype(jnp.bfloat16))


def spread(block, count):
    return jnp.broadcast_to(block[None], (count,) + block.shape)


def exchange(chunks, axis):
    count, rows, cols = chunks.shape
    got = lax.all_to_all(chunks.reshape(count * rows, cols), axis, 0, 0, tiled=True)
    return got.reshape(count, rows, cols)


def on_device(acts, sides, gains, weights, back_acts, back_sides, back_grads):
    sections = lax.axis_size("section")
    count = lax.axis_size("tensor")
    middle = sections // 2
    section_idx = lax.axis_index("section")
    gain = gains[0]
    weight_all = weights[0]
    rows, width = acts[0].shape
    block_cols = weight_all.shape[1]
    lanes = 128
    gain_rows = 2 * width // lanes

    grad_blocks = back_grads[0].reshape(rows, count, block_cols).transpose(1, 0, 2)
    raw = jnp.concatenate([back_acts[0], back_sides[0]], axis=1)
    got_b = exchange(jnp.concatenate([spread(raw, count), grad_blocks], axis=2), "tensor")
    xfloat, _, normed = normalize(acts[0], gain)
    chunks_f = spread(jnp.concatenate([normed, sides[0]], axis=1), count)
    got_b, chunks_f = lax.optimization_barrier((got_b, chunks_f))
    joined_all = exchange(chunks_f, "tensor").reshape(count * rows, 2 * width)

    raw_all = got_b[:, :, : 2 * width].reshape(count * rows, 2 * width)
    grad_cols = got_b[:, :, 2 * width :].reshape(count * rows, block_cols)
    bfloat_all, brinv_all, bnormed_all = normalize(raw_all[:, :width], gain)
    bfused_all = jnp.concatenate([bnormed_all, raw_all[:, width:]], axis=1)
    bhidden = jnp.dot(bfused_all, weight_all, preferred_element_type=jnp.float32)
    dhidden = (grad_cols.astype(jnp.float32) * gelu_slope(bhidden)).astype(jnp.bfloat16)
    contract = (((0,), (0,)), ((), ()))
    weight_grads = lax.dot_general(
        bfused_all, dhidden, contract, preferred_element_type=jnp.float32
    ).astype(jnp.bfloat16)
    across = (((1,), (1,)), ((), ()))
    term = lax.dot_general(
        dhidden, weight_all, across, preferred_element_type=jnp.float32
    ).astype(jnp.bfloat16)
    gain_part = jnp.sum(term[:, :width].astype(jnp.float32) * bfloat_all * brinv_all, axis=0)
    part_hi = gain_part.astype(jnp.bfloat16)
    part_lo = (gain_part - part_hi.astype(jnp.float32)).astype(jnp.bfloat16)
    gain_tile = jnp.concatenate([part_hi, part_lo]).reshape(gain_rows, lanes)
    gain_tile = jnp.pad(gain_tile, ((0, rows - gain_rows), (0, 0)))

    hidden = jnp.dot(joined_all, weight_all, preferred_element_type=jnp.float32)
    update = gelu_value(hidden).astype(jnp.bfloat16)

    chunks_a = jnp.concatenate(
        [term[:, width:].reshape(count, rows, width), update.reshape(count, rows, block_cols)], axis=2
    )
    chunks_a, weight_grads = lax.optimization_barrier((chunks_a, weight_grads))
    got_a = exchange(chunks_a, "tensor")
    dside = jnp.sum(got_a[:, :, :width].astype(jnp.float32), axis=0).astype(jnp.bfloat16)
    update_rows = got_a[:, :, width:].transpose(1, 0, 2).reshape(rows, width)
    out_rows = (xfloat + update_rows.astype(jnp.float32)).astype(jnp.bfloat16)
    received = shifted(out_rows, "section", 1)
    payload = jnp.where(section_idx < middle, out_rows, dside)
    mirrored = lax.ppermute(payload, "section", [(s, sections - 1 - s) for s in range(sections)])

    chunks_b = jnp.concatenate(
        [
            term[:, :width].reshape(count, rows, width),
            jnp.broadcast_to(gain_tile[None], (count, rows, lanes)),
        ],
        axis=2,
    )
    got_a, chunks_b = lax.optimization_barrier((got_a, chunks_b))
    got_b2 = exchange(chunks_b, "tensor")
    dnormed = jnp.sum(got_b2[:, :, :width].astype(jnp.float32), axis=0)
    shares = got_b2[:, :gain_rows, width:].reshape(count, 2 * width).astype(jnp.float32)
    gain_grad = jnp.sum(shares[:, :width] + shares[:, width:], axis=0)

    bfloat, brinv, _ = normalize(back_acts[0], gain)
    scaled = gain * dnormed
    dnorm_in = brinv * scaled - bfloat * brinv * brinv * brinv * jnp.mean(
        scaled * bfloat, axis=-1, keepdims=True
    )
    dx_rows = (back_grads[0].astype(jnp.float32) + dnorm_in).astype(jnp.bfloat16)
    grad_received = shifted(dx_rows, "section", -1)
    return (
        received[None],
        mirrored[None],
        grad_received[None],
        weight_grads[None],
        gain_grad[None],
    )


def solution(mesh):
    placed = (
        P("section", "tensor", None),
        P("section", "tensor", None),
        P("section", None),
        P("section", None, "tensor"),
        P("section", "tensor", None),
        P("section", "tensor", None),
        P("section", "tensor", None),
    )
    return jax.shard_map(
        on_device,
        mesh=mesh,
        in_specs=placed,
        out_specs=(
            P("section", "tensor", None),
            P("section", "tensor", None),
            P("section", "tensor", None),
            P("section", None, "tensor"),
            P("section", None),
        ),
        check_vma=False,
    )
```

```python
import jax
import jax.numpy as jnp
from jax import lax
from jax.sharding import PartitionSpec as P

epsilon = 1e-06
tanh_scale = 0.7978845608028654
cubic_term = 0.044715


def shifted(block, axis, distance):
    devices = range(lax.axis_size(axis))
    route = [((i - distance) % len(devices), i) for i in devices]
    return lax.ppermute(block, axis, route)


def gelu_value(inputs):
    inside = tanh_scale * (inputs + cubic_term * inputs * inputs * inputs)
    return 0.5 * inputs * (1.0 + jnp.tanh(inside))


def gelu_slope(inputs):
    inside = tanh_scale * (inputs + cubic_term * inputs * inputs * inputs)
    bent = jnp.tanh(inside)
    return 0.5 * (1.0 + bent) + 0.5 * inputs * (1.0 - bent * bent) * tanh_scale * (
        1.0 + 3.0 * cubic_term * inputs * inputs
    )


def normalize(rows_in, gain):
    xfloat = rows_in.astype(jnp.float32)
    rinv = lax.rsqrt(jnp.mean(xfloat * xfloat, axis=-1, keepdims=True) + epsilon)
    return (xfloat, rinv, (xfloat * rinv * gain).astype(jnp.bfloat16))


def spread(block, count):
    return jnp.broadcast_to(block[None], (count,) + block.shape)


def exchange(chunks, axis):
    count, rows, cols = chunks.shape
    got = lax.all_to_all(chunks.reshape(count * rows, cols), axis, 0, 0, tiled=True)
    return got.reshape(count, rows, cols)


def on_device(acts, sides, gains, weights, back_acts, back_sides, back_grads):
    sections = lax.axis_size("section")
    count = lax.axis_size("tensor")
    middle = sections // 2
    section_idx = lax.axis_index("section")
    gain = gains[0]
    weight_all = weights[0]
    rows, width = acts[0].shape
    block_cols = weight_all.shape[1]
    lanes = 128
    gain_rows = 2 * width // lanes

    grad_blocks = back_grads[0].reshape(rows, count, block_cols).transpose(1, 0, 2)
    raw = jnp.concatenate([back_acts[0], back_sides[0]], axis=1)
    got_b = exchange(jnp.concatenate([spread(raw, count), grad_blocks], axis=2), "tensor")
    xfloat, _, normed = normalize(acts[0], gain)
    chunks_f = spread(jnp.concatenate([normed, sides[0]], axis=1), count)
    got_b, chunks_f = lax.optimization_barrier((got_b, chunks_f))
    joined_all = exchange(chunks_f, "tensor").reshape(count * rows, 2 * width)

    raw_all = got_b[:, :, : 2 * width].reshape(count * rows, 2 * width)
    grad_cols = got_b[:, :, 2 * width :].reshape(count * rows, block_cols)
    bfloat_all, brinv_all, bnormed_all = normalize(raw_all[:, :width], gain)
    bfused_all = jnp.concatenate([bnormed_all, raw_all[:, width:]], axis=1)
    bhidden = jnp.dot(bfused_all, weight_all, preferred_element_type=jnp.float32)
    dhidden = (grad_cols.astype(jnp.float32) * gelu_slope(bhidden)).astype(jnp.bfloat16)
    contract = (((0,), (0,)), ((), ()))
    weight_grads = lax.dot_general(
        bfused_all, dhidden, contract, preferred_element_type=jnp.float32
    ).astype(jnp.bfloat16)
    across = (((1,), (1,)), ((), ()))
    term = lax.dot_general(
        dhidden, weight_all, across, preferred_element_type=jnp.float32
    ).astype(jnp.bfloat16)
    gain_part = jnp.sum(term[:, :width].astype(jnp.float32) * bfloat_all * brinv_all, axis=0)
    part_hi = gain_part.astype(jnp.bfloat16)
    part_lo = (gain_part - part_hi.astype(jnp.float32)).astype(jnp.bfloat16)
    gain_tile = jnp.concatenate([part_hi, part_lo]).reshape(gain_rows, lanes)
    gain_tile = jnp.pad(gain_tile, ((0, rows - gain_rows), (0, 0)))

    chunks_a = jnp.concatenate(
        [
            term[:, :width].reshape(count, rows, width),
            jnp.broadcast_to(gain_tile[None], (count, rows, lanes)),
        ],
        axis=2,
    )
    chunks_a, weight_grads = lax.optimization_barrier((chunks_a, weight_grads))
    got_a = exchange(chunks_a, "tensor")
    dnormed = jnp.sum(got_a[:, :, :width].astype(jnp.float32), axis=0)
    shares = got_a[:, :gain_rows, width:].reshape(count, 2 * width).astype(jnp.float32)
    gain_grad = jnp.sum(shares[:, :width] + shares[:, width:], axis=0)
    bfloat, brinv, _ = normalize(back_acts[0], gain)
    scaled = gain * dnormed
    dnorm_in = brinv * scaled - bfloat * brinv * brinv * brinv * jnp.mean(
        scaled * bfloat, axis=-1, keepdims=True
    )
    dx_rows = (back_grads[0].astype(jnp.float32) + dnorm_in).astype(jnp.bfloat16)
    grad_received = shifted(dx_rows, "section", -1)

    hidden = jnp.dot(joined_all, weight_all, preferred_element_type=jnp.float32)
    update = gelu_value(hidden).astype(jnp.bfloat16)

    chunks_b = jnp.concatenate(
        [term[:, width:].reshape(count, rows, width), update.reshape(count, rows, block_cols)], axis=2
    )
    got_a, chunks_b = lax.optimization_barrier((got_a, chunks_b))
    got_b2 = exchange(chunks_b, "tensor")
    dside = jnp.sum(got_b2[:, :, :width].astype(jnp.float32), axis=0).astype(jnp.bfloat16)
    update_rows = got_b2[:, :, width:].transpose(1, 0, 2).reshape(rows, width)
    out_rows = (xfloat + update_rows.astype(jnp.float32)).astype(jnp.bfloat16)
    received = shifted(out_rows, "section", 1)
    payload = jnp.where(section_idx < middle, out_rows, dside)
    mirrored = lax.ppermute(payload, "section", [(s, sections - 1 - s) for s in range(sections)])
    return (
        received[None],
        mirrored[None],
        grad_received[None],
        weight_grads[None],
        gain_grad[None],
    )


def solution(mesh):
    placed = (
        P("section", "tensor", None),
        P("section", "tensor", None),
        P("section", None),
        P("section", None, "tensor"),
        P("section", "tensor", None),
        P("section", "tensor", None),
        P("section", "tensor", None),
    )
    return jax.shard_map(
        on_device,
        mesh=mesh,
        in_specs=placed,
        out_specs=(
            P("section", "tensor", None),
            P("section", "tensor", None),
            P("section", "tensor", None),
            P("section", None, "tensor"),
            P("section", None),
        ),
        check_vma=False,
    )
```

```python
import jax
import jax.numpy as jnp
from jax import lax
from jax.sharding import PartitionSpec as P

epsilon = 1e-06
tanh_scale = 0.7978845608028654
cubic_term = 0.044715


def shifted(block, axis, distance):
    devices = range(lax.axis_size(axis))
    route = [((i - distance) % len(devices), i) for i in devices]
    return lax.ppermute(block, axis, route)


def gelu_value(inputs):
    inside = tanh_scale * (inputs + cubic_term * inputs * inputs * inputs)
    return 0.5 * inputs * (1.0 + jnp.tanh(inside))


def gelu_slope(inputs):
    inside = tanh_scale * (inputs + cubic_term * inputs * inputs * inputs)
    bent = jnp.tanh(inside)
    return 0.5 * (1.0 + bent) + 0.5 * inputs * (1.0 - bent * bent) * tanh_scale * (
        1.0 + 3.0 * cubic_term * inputs * inputs
    )


def normalize(rows_in, gain):
    xfloat = rows_in.astype(jnp.float32)
    rinv = lax.rsqrt(jnp.mean(xfloat * xfloat, axis=-1, keepdims=True) + epsilon)
    return (xfloat, rinv, (xfloat * rinv * gain).astype(jnp.bfloat16))


def spread(pieces):
    block = jnp.concatenate(pieces, axis=1)
    return jnp.broadcast_to(block[None], (lax.axis_size("tensor"),) + block.shape)


def exchange(chunks, axis):
    count, rows, cols = chunks.shape
    got = lax.all_to_all(chunks.reshape(count * rows, cols), axis, 0, 0, tiled=True)
    return got.reshape(count, rows, cols)


def on_device(acts, sides, gains, weights, back_acts, back_sides, back_grads):
    sections = lax.axis_size("section")
    count = lax.axis_size("tensor")
    middle = sections // 2
    section_idx = lax.axis_index("section")
    gain = gains[0]
    weight_all = weights[0]
    rows, width = acts[0].shape
    block_cols = weight_all.shape[1]
    lanes = 128
    gain_rows = 2 * width // lanes

    keep = lax.broadcasted_iota(jnp.int32, (count, 1, 1), 0) + section_idx >= 0
    grad_blocks = back_grads[0].reshape(rows, count, block_cols).transpose(1, 0, 2)
    grad_blocks = jnp.pad(grad_blocks, ((0, 0), (0, 0), (2 * width, 0)))
    raw_pad = jnp.zeros((rows, block_cols), jnp.bfloat16)
    is_raw = lax.broadcasted_iota(jnp.int32, (1, 1, 2 * width + block_cols), 2) < 2 * width + 0 * section_idx
    chunks_b = jnp.where(is_raw, spread([back_acts[0], back_sides[0], raw_pad]), grad_blocks)
    got_b = exchange(chunks_b, "tensor")
    xfloat, _, normed = normalize(acts[0], gain)
    chunks_f = jnp.where(keep, spread([normed, sides[0]]), jnp.zeros((), jnp.bfloat16))
    got_b, chunks_f = lax.optimization_barrier((got_b, chunks_f))
    joined_all = exchange(chunks_f, "tensor").reshape(count * rows, 2 * width)

    raw_all = got_b[:, :, : 2 * width].reshape(count * rows, 2 * width)
    grad_cols = got_b[:, :, 2 * width :].reshape(count * rows, block_cols)
    bfloat_all, brinv_all, bnormed_all = normalize(raw_all[:, :width], gain)
    bfused_all = jnp.concatenate([bnormed_all, raw_all[:, width:]], axis=1)
    bhidden = jnp.dot(bfused_all, weight_all, preferred_element_type=jnp.float32)
    dhidden = (grad_cols.astype(jnp.float32) * gelu_slope(bhidden)).astype(jnp.bfloat16)
    contract = (((0,), (0,)), ((), ()))
    weight_grads = lax.dot_general(
        bfused_all, dhidden, contract, preferred_element_type=jnp.float32
    ).astype(jnp.bfloat16)
    across = (((1,), (1,)), ((), ()))
    term = lax.dot_general(
        dhidden, weight_all, across, preferred_element_type=jnp.float32
    ).astype(jnp.bfloat16)
    gain_part = jnp.sum(term[:, :width].astype(jnp.float32) * bfloat_all * brinv_all, axis=0)
    part_hi = gain_part.astype(jnp.bfloat16)
    part_lo = (gain_part - part_hi.astype(jnp.float32)).astype(jnp.bfloat16)
    gain_tile = jnp.concatenate([part_hi, part_lo]).reshape(gain_rows, lanes)
    gain_tile = jnp.pad(gain_tile, ((0, rows - gain_rows), (0, 0)))

    chunks_a = jnp.concatenate(
        [
            term[:, :width].reshape(count, rows, width),
            jnp.broadcast_to(gain_tile[None], (count, rows, lanes)),
        ],
        axis=2,
    )
    chunks_a, weight_grads = lax.optimization_barrier((chunks_a, weight_grads))
    got_a = exchange(chunks_a, "tensor")
    dnormed = jnp.sum(got_a[:, :, :width].astype(jnp.float32), axis=0)
    shares = got_a[:, :gain_rows, width:].reshape(count, 2 * width).astype(jnp.float32)
    gain_grad = jnp.sum(shares[:, :width] + shares[:, width:], axis=0)
    bfloat, brinv, _ = normalize(back_acts[0], gain)
    scaled = gain * dnormed
    dnorm_in = brinv * scaled - bfloat * brinv * brinv * brinv * jnp.mean(
        scaled * bfloat, axis=-1, keepdims=True
    )
    dx_rows = (back_grads[0].astype(jnp.float32) + dnorm_in).astype(jnp.bfloat16)
    grad_received = shifted(dx_rows, "section", -1)

    hidden = jnp.dot(joined_all, weight_all, preferred_element_type=jnp.float32)
    update = gelu_value(hidden).astype(jnp.bfloat16)

    chunks_b = jnp.concatenate(
        [term[:, width:].reshape(count, rows, width), update.reshape(count, rows, block_cols)], axis=2
    )
    got_a, chunks_b = lax.optimization_barrier((got_a, chunks_b))
    got_b2 = exchange(chunks_b, "tensor")
    dside = jnp.sum(got_b2[:, :, :width].astype(jnp.float32), axis=0).astype(jnp.bfloat16)
    update_rows = got_b2[:, :, width:].transpose(1, 0, 2).reshape(rows, width)
    out_rows = (xfloat + update_rows.astype(jnp.float32)).astype(jnp.bfloat16)
    received = shifted(out_rows, "section", 1)
    payload = jnp.where(section_idx < middle, out_rows, dside)
    mirrored = lax.ppermute(payload, "section", [(s, sections - 1 - s) for s in range(sections)])
    return (
        received[None],
        mirrored[None],
        grad_received[None],
        weight_grads[None],
        gain_grad[None],
    )


def solution(mesh):
    placed = (
        P("section", "tensor", None),
        P("section", "tensor", None),
        P("section", None),
        P("section", None, "tensor"),
        P("section", "tensor", None),
        P("section", "tensor", None),
        P("section", "tensor", None),
    )
    return jax.shard_map(
        on_device,
        mesh=mesh,
        in_specs=placed,
        out_specs=(
            P("section", "tensor", None),
            P("section", "tensor", None),
            P("section", "tensor", None),
            P("section", None, "tensor"),
            P("section", None),
        ),
        check_vma=False,
    )
```

```python
import jax
import jax.numpy as jnp
from jax import lax
from jax.sharding import PartitionSpec as P

epsilon = 1e-06
tanh_scale = 0.7978845608028654
cubic_term = 0.044715


def shifted(block, axis, distance):
    devices = range(lax.axis_size(axis))
    route = [((i - distance) % len(devices), i) for i in devices]
    return lax.ppermute(block, axis, route)


def gelu_value(inputs):
    inside = tanh_scale * (inputs + cubic_term * inputs * inputs * inputs)
    return 0.5 * inputs * (1.0 + jnp.tanh(inside))


def gelu_slope(inputs):
    inside = tanh_scale * (inputs + cubic_term * inputs * inputs * inputs)
    bent = jnp.tanh(inside)
    return 0.5 * (1.0 + bent) + 0.5 * inputs * (1.0 - bent * bent) * tanh_scale * (
        1.0 + 3.0 * cubic_term * inputs * inputs
    )


def normalize(rows_in, gain):
    xfloat = rows_in.astype(jnp.float32)
    rinv = lax.rsqrt(jnp.mean(xfloat * xfloat, axis=-1, keepdims=True) + epsilon)
    return (xfloat, rinv, (xfloat * rinv * gain).astype(jnp.bfloat16))


def spread(pieces):
    block = jnp.concatenate(pieces, axis=1)
    return jnp.broadcast_to(block[None], (lax.axis_size("tensor"),) + block.shape)


def exchange(chunks, axis):
    count, rows, cols = chunks.shape
    got = lax.all_to_all(chunks.reshape(count * rows, cols), axis, 0, 0, tiled=True)
    return got.reshape(count, rows, cols)


def on_device(acts, sides, gains, weights, back_acts, back_sides, back_grads):
    sections = lax.axis_size("section")
    count = lax.axis_size("tensor")
    middle = sections // 2
    section_idx = lax.axis_index("section")
    gain = gains[0]
    weight_all = weights[0]
    rows, width = acts[0].shape
    block_cols = weight_all.shape[1]
    lanes = 128
    gain_rows = 2 * width // lanes

    keep = lax.broadcasted_iota(jnp.int32, (count, 1, 1), 0) + section_idx >= 0
    grad_blocks = back_grads[0].reshape(rows, count, block_cols).transpose(1, 0, 2)
    grad_blocks = jnp.pad(grad_blocks, ((0, 0), (0, 0), (2 * width, 0)))
    raw_pad = jnp.zeros((rows, block_cols), jnp.bfloat16)
    is_raw = lax.broadcasted_iota(jnp.int32, (1, 1, 2 * width + block_cols), 2) < 2 * width + 0 * section_idx
    chunks_b = jnp.where(is_raw, spread([back_acts[0], back_sides[0], raw_pad]), grad_blocks)
    got_b = exchange(chunks_b, "tensor")
    xfloat, _, normed = normalize(acts[0], gain)
    chunks_f = jnp.where(keep, spread([normed, sides[0]]), jnp.zeros((), jnp.bfloat16))
    got_b, chunks_f = lax.optimization_barrier((got_b, chunks_f))
    joined_all = exchange(chunks_f, "tensor").reshape(count * rows, 2 * width)

    raw_all = got_b[:, :, : 2 * width].reshape(count * rows, 2 * width)
    grad_cols = got_b[:, :, 2 * width :].reshape(count * rows, block_cols)
    bfloat_all, brinv_all, bnormed_all = normalize(raw_all[:, :width], gain)
    bfused_all = jnp.concatenate([bnormed_all, raw_all[:, width:]], axis=1)
    bhidden = jnp.dot(bfused_all, weight_all, preferred_element_type=jnp.float32)
    dhidden = (grad_cols.astype(jnp.float32) * gelu_slope(bhidden)).astype(jnp.bfloat16)
    contract = (((0,), (0,)), ((), ()))
    across = (((1,), (1,)), ((), ()))
    term = lax.dot_general(
        dhidden, weight_all, across, preferred_element_type=jnp.float32
    ).astype(jnp.bfloat16)
    gain_part = jnp.sum(term[:, :width].astype(jnp.float32) * bfloat_all * brinv_all, axis=0)
    part_hi = gain_part.astype(jnp.bfloat16)
    part_lo = (gain_part - part_hi.astype(jnp.float32)).astype(jnp.bfloat16)
    gain_tile = jnp.concatenate([part_hi, part_lo]).reshape(gain_rows, lanes)
    gain_tile = jnp.pad(gain_tile, ((0, rows - gain_rows), (0, 0)))

    chunks_a = jnp.concatenate(
        [
            term[:, :width].reshape(count, rows, width),
            jnp.broadcast_to(gain_tile[None], (count, rows, lanes)),
        ],
        axis=2,
    )
    got_a = exchange(chunks_a, "tensor")
    dnormed = jnp.sum(got_a[:, :, :width].astype(jnp.float32), axis=0)
    shares = got_a[:, :gain_rows, width:].reshape(count, 2 * width).astype(jnp.float32)
    gain_grad = jnp.sum(shares[:, :width] + shares[:, width:], axis=0)
    bfloat, brinv, _ = normalize(back_acts[0], gain)
    scaled = gain * dnormed
    dnorm_in = brinv * scaled - bfloat * brinv * brinv * brinv * jnp.mean(
        scaled * bfloat, axis=-1, keepdims=True
    )
    dx_rows = (back_grads[0].astype(jnp.float32) + dnorm_in).astype(jnp.bfloat16)
    grad_received = shifted(dx_rows, "section", -1)

    hidden = jnp.dot(joined_all, weight_all, preferred_element_type=jnp.float32)
    update = gelu_value(hidden).astype(jnp.bfloat16)

    chunks_b = jnp.concatenate(
        [term[:, width:].reshape(count, rows, width), update.reshape(count, rows, block_cols)], axis=2
    )
    got_a, chunks_b = lax.optimization_barrier((got_a, chunks_b))
    got_b2 = exchange(chunks_b, "tensor")
    dside = jnp.sum(got_b2[:, :, :width].astype(jnp.float32), axis=0).astype(jnp.bfloat16)
    update_rows = got_b2[:, :, width:].transpose(1, 0, 2).reshape(rows, width)
    out_rows = (xfloat + update_rows.astype(jnp.float32)).astype(jnp.bfloat16)
    received = shifted(out_rows, "section", 1)
    payload = jnp.where(section_idx < middle, out_rows, dside)
    mirrored = lax.ppermute(payload, "section", [(s, sections - 1 - s) for s in range(sections)])
    got_b2, bfused_all, dhidden = lax.optimization_barrier((got_b2, bfused_all, dhidden))
    weight_grads = lax.dot_general(
        bfused_all, dhidden, contract, preferred_element_type=jnp.float32
    ).astype(jnp.bfloat16)
    return (
        received[None],
        mirrored[None],
        grad_received[None],
        weight_grads[None],
        gain_grad[None],
    )


def solution(mesh):
    placed = (
        P("section", "tensor", None),
        P("section", "tensor", None),
        P("section", None),
        P("section", None, "tensor"),
        P("section", "tensor", None),
        P("section", "tensor", None),
        P("section", "tensor", None),
    )
    return jax.shard_map(
        on_device,
        mesh=mesh,
        in_specs=placed,
        out_specs=(
            P("section", "tensor", None),
            P("section", "tensor", None),
            P("section", "tensor", None),
            P("section", None, "tensor"),
            P("section", None),
        ),
        check_vma=False,
    )
```

```python
import jax
import jax.numpy as jnp
from jax import lax
from jax.sharding import PartitionSpec as P

epsilon = 1e-06
tanh_scale = 0.7978845608028654
cubic_term = 0.044715


def shifted(block, axis, distance):
    devices = range(lax.axis_size(axis))
    route = [((i - distance) % len(devices), i) for i in devices]
    return lax.ppermute(block, axis, route)


def gelu_value(inputs):
    inside = tanh_scale * (inputs + cubic_term * inputs * inputs * inputs)
    return 0.5 * inputs * (1.0 + jnp.tanh(inside))


def gelu_slope(inputs):
    inside = tanh_scale * (inputs + cubic_term * inputs * inputs * inputs)
    bent = jnp.tanh(inside)
    return 0.5 * (1.0 + bent) + 0.5 * inputs * (1.0 - bent * bent) * tanh_scale * (
        1.0 + 3.0 * cubic_term * inputs * inputs
    )


def normalize(rows_in, gain):
    xfloat = rows_in.astype(jnp.float32)
    rinv = lax.rsqrt(jnp.mean(xfloat * xfloat, axis=-1, keepdims=True) + epsilon)
    return (xfloat, rinv, (xfloat * rinv * gain).astype(jnp.bfloat16))


def spread(pieces):
    block = jnp.concatenate(pieces, axis=1)
    return jnp.broadcast_to(block[None], (lax.axis_size("tensor"),) + block.shape)


def exchange(chunks, axis):
    count, rows, cols = chunks.shape
    got = lax.all_to_all(chunks.reshape(count * rows, cols), axis, 0, 0, tiled=True)
    return got.reshape(count, rows, cols)


def on_device(acts, sides, gains, weights, back_acts, back_sides, back_grads):
    sections = lax.axis_size("section")
    count = lax.axis_size("tensor")
    middle = sections // 2
    section_idx = lax.axis_index("section")
    gain = gains[0]
    weight_all = weights[0]
    rows, width = acts[0].shape
    block_cols = weight_all.shape[1]
    lanes = 128
    gain_rows = 2 * width // lanes

    keep = lax.broadcasted_iota(jnp.int32, (count, 1, 1), 0) + section_idx >= 0
    grad_blocks = back_grads[0].reshape(rows, count, block_cols).transpose(1, 0, 2)
    grad_blocks = jnp.pad(grad_blocks, ((0, 0), (0, 0), (2 * width, 0)))
    raw_pad = jnp.zeros((rows, block_cols), jnp.bfloat16)
    is_raw = lax.broadcasted_iota(jnp.int32, (1, 1, 2 * width + block_cols), 2) < 2 * width + 0 * section_idx
    chunks_b = jnp.where(is_raw, spread([back_acts[0], back_sides[0], raw_pad]), grad_blocks)
    got_b = exchange(chunks_b, "tensor")
    xfloat, _, normed = normalize(acts[0], gain)
    chunks_f = jnp.where(keep, spread([normed, sides[0]]), jnp.zeros((), jnp.bfloat16))
    got_b, chunks_f = lax.optimization_barrier((got_b, chunks_f))
    joined_all = exchange(chunks_f, "tensor").reshape(count * rows, 2 * width)

    raw_all = got_b[:, :, : 2 * width].reshape(count * rows, 2 * width)
    grad_cols = got_b[:, :, 2 * width :].reshape(count * rows, block_cols)
    bfloat_all, brinv_all, bnormed_all = normalize(raw_all[:, :width], gain)
    bfused_all = jnp.concatenate([bnormed_all, raw_all[:, width:]], axis=1)
    bhidden = jnp.dot(bfused_all, weight_all, preferred_element_type=jnp.float32)
    dhidden = (grad_cols.astype(jnp.float32) * gelu_slope(bhidden)).astype(jnp.bfloat16)
    contract = (((0,), (0,)), ((), ()))
    weight_grads = lax.dot_general(
        bfused_all, dhidden, contract, preferred_element_type=jnp.float32
    ).astype(jnp.bfloat16)
    across = (((1,), (1,)), ((), ()))
    term = lax.dot_general(
        dhidden, weight_all, across, preferred_element_type=jnp.float32
    ).astype(jnp.bfloat16)
    gain_part = jnp.sum(term[:, :width].astype(jnp.float32) * bfloat_all * brinv_all, axis=0)
    part_hi = gain_part.astype(jnp.bfloat16)
    part_lo = (gain_part - part_hi.astype(jnp.float32)).astype(jnp.bfloat16)
    gain_tile = jnp.concatenate([part_hi, part_lo]).reshape(gain_rows, lanes)
    gain_tile = jnp.pad(gain_tile, ((0, rows - gain_rows), (0, 0)))

    chunks_a = jnp.concatenate(
        [
            term.reshape(count, rows, 2 * width),
            jnp.broadcast_to(gain_tile[None], (count, rows, lanes)),
        ],
        axis=2,
    )
    chunks_a, weight_grads = lax.optimization_barrier((chunks_a, weight_grads))
    got_a = exchange(chunks_a, "tensor")
    dnormed = jnp.sum(got_a[:, :, :width].astype(jnp.float32), axis=0)
    dside = jnp.sum(got_a[:, :, width : 2 * width].astype(jnp.float32), axis=0).astype(jnp.bfloat16)
    shares = got_a[:, :gain_rows, 2 * width :].reshape(count, 2 * width).astype(jnp.float32)
    gain_grad = jnp.sum(shares[:, :width] + shares[:, width:], axis=0)
    bfloat, brinv, _ = normalize(back_acts[0], gain)
    scaled = gain * dnormed
    dnorm_in = brinv * scaled - bfloat * brinv * brinv * brinv * jnp.mean(
        scaled * bfloat, axis=-1, keepdims=True
    )
    dx_rows = (back_grads[0].astype(jnp.float32) + dnorm_in).astype(jnp.bfloat16)
    grad_received = shifted(dx_rows, "section", -1)

    hidden = jnp.dot(joined_all, weight_all, preferred_element_type=jnp.float32)
    update = gelu_value(hidden).astype(jnp.bfloat16)

    chunks_u = update.reshape(count, rows, block_cols)
    got_a, chunks_u = lax.optimization_barrier((got_a, chunks_u))
    got_u = exchange(chunks_u, "tensor")
    update_rows = got_u.transpose(1, 0, 2).reshape(rows, width)
    out_rows = (xfloat + update_rows.astype(jnp.float32)).astype(jnp.bfloat16)
    received = shifted(out_rows, "section", 1)
    payload = jnp.where(section_idx < middle, out_rows, dside)
    mirrored = lax.ppermute(payload, "section", [(s, sections - 1 - s) for s in range(sections)])
    return (
        received[None],
        mirrored[None],
        grad_received[None],
        weight_grads[None],
        gain_grad[None],
    )


def solution(mesh):
    placed = (
        P("section", "tensor", None),
        P("section", "tensor", None),
        P("section", None),
        P("section", None, "tensor"),
        P("section", "tensor", None),
        P("section", "tensor", None),
        P("section", "tensor", None),
    )
    return jax.shard_map(
        on_device,
        mesh=mesh,
        in_specs=placed,
        out_specs=(
            P("section", "tensor", None),
            P("section", "tensor", None),
            P("section", "tensor", None),
            P("section", None, "tensor"),
            P("section", None),
        ),
        check_vma=False,
    )
```

```python
import jax
import jax.numpy as jnp
from jax import lax
from jax.sharding import PartitionSpec as P

epsilon = 1e-06
tanh_scale = 0.7978845608028654
cubic_term = 0.044715


def shifted(block, axis, distance):
    devices = range(lax.axis_size(axis))
    route = [((i - distance) % len(devices), i) for i in devices]
    return lax.ppermute(block, axis, route)


def gelu_value(inputs):
    inside = tanh_scale * (inputs + cubic_term * inputs * inputs * inputs)
    return 0.5 * inputs * (1.0 + jnp.tanh(inside))


def gelu_slope(inputs):
    inside = tanh_scale * (inputs + cubic_term * inputs * inputs * inputs)
    bent = jnp.tanh(inside)
    return 0.5 * (1.0 + bent) + 0.5 * inputs * (1.0 - bent * bent) * tanh_scale * (
        1.0 + 3.0 * cubic_term * inputs * inputs
    )


def normalize(rows_in, gain):
    xfloat = rows_in.astype(jnp.float32)
    rinv = lax.rsqrt(jnp.mean(xfloat * xfloat, axis=-1, keepdims=True) + epsilon)
    return (xfloat, rinv, (xfloat * rinv * gain).astype(jnp.bfloat16))


def spread(pieces):
    block = jnp.concatenate(pieces, axis=1)
    return jnp.broadcast_to(block[None], (lax.axis_size("tensor"),) + block.shape)


def exchange(chunks, axis):
    count, rows, cols = chunks.shape
    got = lax.all_to_all(chunks.reshape(count * rows, cols), axis, 0, 0, tiled=True)
    return got.reshape(count, rows, cols)


def on_device(acts, sides, gains, weights, back_acts, back_sides, back_grads):
    sections = lax.axis_size("section")
    count = lax.axis_size("tensor")
    middle = sections // 2
    section_idx = lax.axis_index("section")
    gain = gains[0]
    weight_all = weights[0]
    rows, width = acts[0].shape
    block_cols = weight_all.shape[1]
    lanes = 128
    gain_rows = 2 * width // lanes

    keep = lax.broadcasted_iota(jnp.int32, (count, 1, 1), 0) + section_idx >= 0
    grad_blocks = back_grads[0].reshape(rows, count, block_cols).transpose(1, 0, 2)
    grad_blocks = jnp.pad(grad_blocks, ((0, 0), (0, 0), (2 * width, 0)))
    raw_pad = jnp.zeros((rows, block_cols), jnp.bfloat16)
    is_raw = lax.broadcasted_iota(jnp.int32, (1, 1, 2 * width + block_cols), 2) < 2 * width + 0 * section_idx
    chunks_b = jnp.where(is_raw, spread([back_acts[0], back_sides[0], raw_pad]), grad_blocks)
    got_b = exchange(chunks_b, "tensor")
    xfloat, _, normed = normalize(acts[0], gain)
    chunks_f = jnp.where(keep, spread([normed, sides[0]]), jnp.zeros((), jnp.bfloat16))
    got_b, chunks_f = lax.optimization_barrier((got_b, chunks_f))
    joined_all = exchange(chunks_f, "tensor").reshape(count * rows, 2 * width)

    raw_all = got_b[:, :, : 2 * width].reshape(count * rows, 2 * width)
    grad_cols = got_b[:, :, 2 * width :].reshape(count * rows, block_cols)
    bfloat_all, brinv_all, bnormed_all = normalize(raw_all[:, :width], gain)
    bfused_all = jnp.concatenate([bnormed_all, raw_all[:, width:]], axis=1)
    bhidden = jnp.dot(bfused_all, weight_all, preferred_element_type=jnp.float32)
    dhidden = (grad_cols.astype(jnp.float32) * gelu_slope(bhidden)).astype(jnp.bfloat16)
    contract = (((0,), (0,)), ((), ()))
    weight_grads = lax.dot_general(
        bfused_all, dhidden, contract, preferred_element_type=jnp.float32
    ).astype(jnp.bfloat16)
    across = (((1,), (1,)), ((), ()))
    term = lax.dot_general(
        dhidden, weight_all, across, preferred_element_type=jnp.float32
    ).astype(jnp.bfloat16)
    gain_part = jnp.sum(term[:, :width].astype(jnp.float32) * bfloat_all * brinv_all, axis=0)
    part_hi = gain_part.astype(jnp.bfloat16)
    part_lo = (gain_part - part_hi.astype(jnp.float32)).astype(jnp.bfloat16)
    gain_tile = jnp.concatenate([part_hi, part_lo]).reshape(gain_rows, lanes)
    gain_tile = jnp.pad(gain_tile, ((0, rows - gain_rows), (0, 0)))

    chunks_a = term.reshape(count, rows, 2 * width)
    chunks_a, weight_grads = lax.optimization_barrier((chunks_a, weight_grads))
    got_a = exchange(chunks_a, "tensor")
    dnormed = jnp.sum(got_a[:, :, :width].astype(jnp.float32), axis=0)
    dside = jnp.sum(got_a[:, :, width : 2 * width].astype(jnp.float32), axis=0).astype(jnp.bfloat16)
    bfloat, brinv, _ = normalize(back_acts[0], gain)
    scaled = gain * dnormed
    dnorm_in = brinv * scaled - bfloat * brinv * brinv * brinv * jnp.mean(
        scaled * bfloat, axis=-1, keepdims=True
    )
    dx_rows = (back_grads[0].astype(jnp.float32) + dnorm_in).astype(jnp.bfloat16)
    grad_received = shifted(dx_rows, "section", -1)

    hidden = jnp.dot(joined_all, weight_all, preferred_element_type=jnp.float32)
    update = gelu_value(hidden).astype(jnp.bfloat16)

    chunks_u = jnp.concatenate(
        [update.reshape(count, rows, block_cols), jnp.broadcast_to(gain_tile[None], (count, rows, lanes))],
        axis=2,
    )
    got_a, chunks_u = lax.optimization_barrier((got_a, chunks_u))
    got_u = exchange(chunks_u, "tensor")
    update_rows = got_u[:, :, :block_cols].transpose(1, 0, 2).reshape(rows, width)
    shares = got_u[:, :gain_rows, block_cols:].reshape(count, 2 * width).astype(jnp.float32)
    gain_grad = jnp.sum(shares[:, :width] + shares[:, width:], axis=0)
    out_rows = (xfloat + update_rows.astype(jnp.float32)).astype(jnp.bfloat16)
    received = shifted(out_rows, "section", 1)
    payload = jnp.where(section_idx < middle, out_rows, dside)
    mirrored = lax.ppermute(payload, "section", [(s, sections - 1 - s) for s in range(sections)])
    return (
        received[None],
        mirrored[None],
        grad_received[None],
        weight_grads[None],
        gain_grad[None],
    )


def solution(mesh):
    placed = (
        P("section", "tensor", None),
        P("section", "tensor", None),
        P("section", None),
        P("section", None, "tensor"),
        P("section", "tensor", None),
        P("section", "tensor", None),
        P("section", "tensor", None),
    )
    return jax.shard_map(
        on_device,
        mesh=mesh,
        in_specs=placed,
        out_specs=(
            P("section", "tensor", None),
            P("section", "tensor", None),
            P("section", "tensor", None),
            P("section", None, "tensor"),
            P("section", None),
        ),
        check_vma=False,
    )
```
